128 devices in a mesh: section: 8 (over x, core), wafer: 4 (over y), sub: 4 (over z).
Axes of the slice: x: 4, y: 4, z: 4, core: 2. Of those that a mesh axis runs over, the one named last changes fastest.
Arguments:
- tod: float32 [1, 256, 8192], P(None, 'wafer', ('section', 'sub')), may hold values from -6 to 6
- templates: float32 [1, 256, 8192], P(None, 'wafer', ('section', 'sub'))
- det_weight: float32 [256], P('wafer'), may hold values from 0.3 to 3
- pixel: int32 [1, 256, 8192], P(None, 'wafer', ('section', 'sub')), may hold values from 0 to 511
- hitlist: int32 [1, 64, 512], P(None, 'wafer', ('section', 'sub')), may hold values from 0 to 127, as said below
- counts: int32 [1, 64, 32], P(None, 'wafer', ('section', 'sub')), may hold values from 2 to 16
Outputs:
- sky_map: float32 [8192], P(('wafer', 'sub'))
The draws below stay inside these ranges and needn't reach their ends.
Inputs may be any that keep to these rules, and one draw needn't show every extreme that they name: `hitlist`: for each micro-batch, source device and tile, the live slots name distinct blocks of that source, and no block is named by live slots of two tiles; in each micro-batch exactly one tile has a full hit list (all 16 slots live) from every source device.
All inputs are finite; a program needn't handle non-finite values.
Results may differ from the reference program's by a relative error of at most 0.0003.
Values sent between devices are 32-bit elements; how exact they have to be, the bound alone decides.
No kernel may reach another device: no remote copies, remote signals or barrier semaphores. Data moves between devices by JAX's collectives and lax.ppermute only.
A program may use at most 64 MiB of HBM per device.

```python
import math
import jax
import jax.numpy as jnp
import numpy as np
from jax import lax

TEMPL = 64
DET_W = 64
SAMP_L = 256
MB = 1
BL = 128
TILE = 512
DETS = 256
SAMPLES = 8192
OWNERS = 16
NBL = 128
CAPB = 16
HOT = 1
NPIX = 8192
N_SECTION = 8
N_WAFER = 4
N_SUB = 4


def hit_plan(key):
    block_count = N_SECTION * N_SUB
    key_hot = jax.random.fold_in(key, 101)
    key_other = jax.random.fold_in(key, 102)
    key_mult = jax.random.fold_in(key, 103)
    key_shift = jax.random.fold_in(key, 104)
    ranks = jax.vmap(lambda subkey: jax.random.permutation(subkey, OWNERS))(jax.random.split(key_hot, MB))
    hot_mask = ranks < HOT
    lowest = max(1, CAPB // 8)
    highest = max(lowest, 7 * CAPB // 16)
    others = jax.random.randint(key_other, (MB, N_WAFER, block_count, OWNERS), lowest, highest + 1)
    live_counts = jnp.where(hot_mask[:, None, None, :], CAPB, others).astype(jnp.int32)
    offsets = jnp.cumsum(live_counts, axis=-1) - live_counts
    slot_ids = jnp.arange(CAPB, dtype=jnp.int32)
    position = (offsets[..., None] + slot_ids) % NBL
    multiplier = 2 * jax.random.randint(key_mult, (MB, N_WAFER, block_count, 1, 1), 0, NBL // 2) + 1
    shift_by = jax.random.randint(key_shift, (MB, N_WAFER, block_count, 1, 1), 0, NBL)
    block_ids = (multiplier * position + shift_by) % NBL
    count_out = live_counts.transpose(0, 1, 3, 2).reshape(MB, N_WAFER * OWNERS, block_count)
    hit_out = block_ids.transpose(0, 1, 3, 2, 4).reshape(MB, N_WAFER * OWNERS, block_count * CAPB)
    return (hit_out.astype(jnp.int32), count_out.astype(jnp.int32))


def draw_hitlist(key, part):
    return hit_plan(key)[0]


def draw_counts(key, part):
    return hit_plan(key)[1]


def draw_templates(key, part):
    rows = N_WAFER * TEMPL
    key_noise = jax.random.fold_in(key, 201)
    key_scale = jax.random.fold_in(key, 202)
    key_mix = jax.random.fold_in(key, 203)
    key_common = jax.random.fold_in(key, 204)
    noise = jax.random.normal(key_noise, (MB, rows, SAMPLES), jnp.float32)
    share = 0.7
    scale = jnp.exp(jax.random.uniform(key_scale, (MB, rows, 1), jnp.float32, jnp.log(0.3), jnp.log(3.0)))
    mix = jax.random.normal(key_mix, (MB, rows, 1), jnp.float32) * share
    common = jax.random.normal(key_common, (MB, N_WAFER, 1, SAMPLES), jnp.float32)
    common = jnp.broadcast_to(common, (MB, N_WAFER, TEMPL, SAMPLES)).reshape(MB, rows, SAMPLES)
    return scale * noise + mix * common


def place_ends(result, key, least, largest):
    longest = result.shape.index(max(result.shape))
    spots = []
    for shift in (0, 1):
        where = [jax.random.randint(jax.random.fold_in(key, axis), (), 0, length) for axis, length in enumerate(result.shape)]
        where[longest] = (where[longest] + shift) % result.shape[longest]
        spots.append(tuple(where))
    return result.at[spots[0]].set(least).at[spots[1]].set(largest)


def block_levels(rng, dims, shards, smallest, top_value):
    def one(dim, shards_of):
        steps = jax.random.uniform(jax.random.fold_in(jax.random.fold_in(rng, 6), dim), (shards_of,), jnp.float32, smallest / len(shards), top_value / len(shards))
        return jnp.repeat(jnp.exp(steps), dims[dim] // shards_of).reshape((-1,) + (1,) * (len(dims) - dim - 1))

    level = one(*shards[0])
    for cut in shards[1:]:
        level = level * one(*cut)
    return level


def cumulative_ranks(amount, slope):
    weights = [(1 << 20) // math.isqrt(standing ** slope) + 1 for standing in range(1, amount + 1)]
    scale = 1 + sum(weights) // (1 << 30)
    return np.cumsum(np.array([max(1, weight // scale) for weight in weights]))


def skewed_ids(own_key, shape, amount, slope):
    grid = cumulative_ranks(amount, slope)
    lot = jax.random.randint(jax.random.fold_in(own_key, 1), shape, 0, int(grid[amount - 1]))
    rank = jnp.searchsorted(jnp.asarray(grid, jnp.int32), lot, side="right")
    return jax.random.permutation(jax.random.fold_in(own_key, 2), amount)[rank].astype(jnp.int32)


def scatter_about(rng, dims, deviation, most, pieces=(), held_as=jnp.bfloat16):
    array = jax.random.normal(rng, dims, jnp.float32) * deviation
    if len(pieces) > 0:
        array = block_levels(rng, dims, pieces, -0.22, 0.18) * array
    return jnp.clip(array, min=-most, max=most).astype(held_as)


def setup_inputs(seed: int = 0) -> dict:
    key_of = jax.random.split(jax.random.key(seed), 7)
    return {
        "tod": scatter_about(key_of[0], (MB, DETS, SAMPLES), 1.0, 6.0, ((1, 4), (2, 32)), jnp.float32),
        "templates": draw_templates(jax.random.fold_in(key_of[6], 71), 0),
        "det_weight": jnp.clip(jnp.exp(math.log(3.0) - 2.3025851 * jax.random.uniform(key_of[2], (DETS,), jnp.float32) ** block_levels(key_of[2], (DETS,), ((0, 4),), -0.2, 0.2)), 0.3, 3.0),
        "pixel": place_ends(skewed_ids(key_of[3], (MB, DETS, SAMPLES), TILE, 3), jax.random.fold_in(key_of[3], 3), 0, TILE - 1).astype(jnp.int32),
        "hitlist": draw_hitlist(jax.random.fold_in(key_of[6], 71), 0),
        "counts": draw_counts(jax.random.fold_in(key_of[6], 71), 0),
    }


def pick_rows(source_rows, row_index):
    return source_rows[row_index]

def solve_fit(factor_one, proj_one):
    return jax.scipy.linalg.cho_solve((factor_one, True), proj_one)

def reference(tod, templates, det_weight, pixel, hitlist, counts):
    block_count = N_SECTION * N_SUB
    per_det = SAMP_L // BL
    owner_base = jnp.arange(OWNERS, dtype=jnp.int32) * TILE
    slot_ids = jnp.arange(CAPB, dtype=jnp.int32)
    num_map = jnp.zeros((NPIX,), jnp.float32)
    wgt_map = jnp.zeros((NPIX,), jnp.float32)
    block_weight = jnp.repeat(det_weight.reshape(N_WAFER, DET_W), per_det, axis=1)
    for batch_index in range(MB):
        streams = tod[batch_index].reshape(N_WAFER, DET_W, SAMPLES)
        modes = templates[batch_index].reshape(N_WAFER, TEMPL, SAMPLES)
        gram = jnp.einsum('wks,wls->wkl', modes, modes, precision=lax.Precision.HIGHEST)
        proj = jnp.einsum('wks,wds->wkd', modes, streams, precision=lax.Precision.HIGHEST)
        factor = jnp.linalg.cholesky(gram)
        coef = jax.vmap(solve_fit)(factor, proj)
        filtered = streams - jnp.einsum('wkd,wks->wds', coef, modes, precision=lax.Precision.HIGHEST)
        weighted = filtered * det_weight.reshape(N_WAFER, DET_W, 1)
        value_blocks = weighted.reshape(N_WAFER, DET_W, block_count, per_det, BL)
        value_blocks = value_blocks.transpose(0, 2, 1, 3, 4).reshape(N_WAFER, block_count, NBL, BL)
        pixel_blocks = pixel[batch_index].reshape(N_WAFER, DET_W, block_count, per_det, BL)
        pixel_blocks = pixel_blocks.transpose(0, 2, 1, 3, 4).reshape(N_WAFER, block_count, NBL, BL)
        hit_rows = hitlist[batch_index].reshape(N_WAFER, OWNERS, block_count, CAPB).transpose(0, 2, 1, 3)
        live_counts = counts[batch_index].reshape(N_WAFER, OWNERS, block_count).transpose(0, 2, 1)

        def one_wafer(carry, inputs_now):
            num_now, wgt_now = carry
            wafer_values, wafer_pixels, wafer_weight, wafer_hits, wafer_counts = inputs_now
            live_slots = slot_ids[None, None, :] < wafer_counts[:, :, None]
            values = jax.vmap(pick_rows)(wafer_values, wafer_hits)
            pixels = jax.vmap(pick_rows)(wafer_pixels, wafer_hits)
            values = jnp.where(live_slots[..., None], values, 0.0)
            weights = jnp.where(live_slots, wafer_weight[wafer_hits], 0.0)
            weights = jnp.broadcast_to(weights[..., None], values.shape)
            keys = (owner_base[None, :, None, None] + pixels).astype(jnp.int32)
            num_now = num_now + jax.ops.segment_sum(values.reshape(-1), keys.reshape(-1), num_segments=NPIX)
            wgt_now = wgt_now + jax.ops.segment_sum(weights.reshape(-1), keys.reshape(-1), num_segments=NPIX)
            return ((num_now, wgt_now), None)
        (num_map, wgt_map), unused = lax.scan(one_wafer, (num_map, wgt_map), (value_blocks, pixel_blocks, block_weight, hit_rows, live_counts))
    return num_map / jnp.maximum(wgt_map, 1.0)
```

```python
import jax
import jax.numpy as jnp
from jax import lax
from jax.sharding import PartitionSpec as P

BL = 128
TILE = 512


def bin_block(values, pixels, weights, tile_size):
    upper_count = tile_size // 128
    row_count = values.shape[0]
    upper_part = pixels // 128
    lower_part = pixels % 128
    upper_hot = (
        lax.broadcasted_iota(jnp.int32, (upper_count, row_count), 0) == upper_part[None, :]
    ).astype(jnp.float32)
    lower_hot = (
        lax.broadcasted_iota(jnp.int32, (row_count, 128), 1) == lower_part[:, None]
    ).astype(jnp.float32)
    stacked = jnp.concatenate([upper_hot * values[None, :], upper_hot * weights[None, :]], axis=0)
    binned = jnp.dot(
        stacked, lower_hot, precision=lax.Precision.HIGHEST, preferred_element_type=jnp.float32
    )
    return (binned[:upper_count].reshape(-1), binned[upper_count:].reshape(-1))


def all_sum(x, axes):
    for axis in axes:
        size = lax.axis_size(axis)
        bit = 1
        while bit < size:
            x = x + lax.ppermute(x, axis, [(i, i ^ bit) for i in range(size)])
            bit *= 2
    return x


def shards(tod, templates, det_weight, pixel, hitlist, counts):
    samp_local = tod.shape[2]
    owners = hitlist.shape[1]
    slots = hitlist.shape[2]
    per_det = samp_local // BL
    tile_size = TILE
    slot_ids = lax.broadcasted_iota(jnp.int32, (owners, slots), 1)
    block_weight = jnp.repeat(det_weight, per_det)
    num_tile = jnp.zeros((tile_size,), jnp.float32)
    wgt_tile = jnp.zeros((tile_size,), jnp.float32)

    def add_source(carry, inputs_now):
        num_part, wgt_part = bin_block(inputs_now[0], inputs_now[1], inputs_now[2], tile_size)
        return ((carry[0] + num_part, carry[1] + wgt_part), None)

    template_rows = templates[0]
    streams = tod[0]
    gram_sum = lax.dot_general(
        template_rows,
        template_rows,
        (((1,), (1,)), ((), ())),
        precision=lax.Precision.HIGHEST,
        preferred_element_type=jnp.float32,
    )
    projection = lax.dot_general(
        template_rows,
        streams,
        (((1,), (1,)), ((), ())),
        precision=lax.Precision.HIGHEST,
        preferred_element_type=jnp.float32,
    )
    joined = all_sum(jnp.concatenate([gram_sum, projection], axis=1), ("section", "sub"))
    gram_sum, projection = joined[:, : gram_sum.shape[1]], joined[:, gram_sum.shape[1] :]
    factor = jnp.linalg.cholesky(gram_sum)
    coef_fit = jax.scipy.linalg.cho_solve((factor, True), projection)
    removed = lax.dot_general(
        coef_fit,
        template_rows,
        (((0,), (0,)), ((), ())),
        precision=lax.Precision.HIGHEST,
        preferred_element_type=jnp.float32,
    )
    filtered = streams - removed
    weighted = (filtered * det_weight[:, None]).reshape(-1, BL)
    pixel_blocks = pixel[0].reshape(-1, BL)
    hit_rows = hitlist[0]
    live_slots = slot_ids < counts[0]
    send_values = jnp.where(live_slots[:, :, None], weighted[hit_rows], 0.0)
    send_pixels = jnp.where(live_slots[:, :, None], pixel_blocks[hit_rows], 0)
    send_weights = jnp.where(live_slots, block_weight[hit_rows], 0.0)
    got_values = lax.all_to_all(
        send_values, ("wafer", "sub"), split_axis=0, concat_axis=0, tiled=True
    )
    got_pixels = lax.all_to_all(
        send_pixels, ("wafer", "sub"), split_axis=0, concat_axis=0, tiled=True
    )
    got_weights = lax.all_to_all(
        send_weights, ("wafer", "sub"), split_axis=0, concat_axis=0, tiled=True
    )
    full_weights = jnp.broadcast_to(got_weights[..., None], got_values.shape)
    row_len = slots * BL
    (num_tile, wgt_tile), unused = lax.scan(
        add_source,
        (num_tile, wgt_tile),
        (
            got_values.reshape(-1, row_len),
            got_pixels.reshape(-1, row_len),
            full_weights.reshape(-1, row_len),
        ),
    )
    both = all_sum(jnp.stack([num_tile, wgt_tile]), ("section",))
    num_tile, wgt_tile = both[0], both[1]
    return num_tile / jnp.maximum(wgt_tile, 1.0)


def solution(mesh):
    placed = (
        P(None, "wafer", ("section", "sub")),
        P(None, "wafer", ("section", "sub")),
        P("wafer"),
        P(None, "wafer", ("section", "sub")),
        P(None, "wafer", ("section", "sub")),
        P(None, "wafer", ("section", "sub")),
    )
    return jax.shard_map(
        shards, mesh=mesh, in_specs=placed, out_specs=P(("wafer", "sub")), check_vma=False
    )
```

```python
import jax
import jax.numpy as jnp
from jax import lax
from jax.sharding import PartitionSpec as P

BL = 128
TILE = 512
HIGHEST = lax.Precision.HIGHEST


def all_sum(x, axes):
    for axis in axes:
        size = lax.axis_size(axis)
        bit = 1
        while bit < size:
            x = x + lax.ppermute(x, axis, [(i, i ^ bit) for i in range(size)])
            bit *= 2
    return x


def bin_tiles(values, pixels, weights, tile_of_sample, owners):
    uppers = owners * (TILE // 128)
    upper = jnp.where(tile_of_sample >= 0, tile_of_sample * (TILE // 128) + pixels // 128, -1).reshape(-1)
    lower = (pixels % 128).reshape(-1)
    count = upper.shape[0]
    upper_hot = (lax.broadcasted_iota(jnp.int32, (uppers, count), 0) == upper[None, :]).astype(jnp.float32)
    lower_hot = (lax.broadcasted_iota(jnp.int32, (128, count), 0) == lower[None, :]).astype(jnp.float32)
    stacked = jnp.concatenate(
        [upper_hot * values.reshape(1, -1), upper_hot * weights.reshape(1, -1)], axis=0
    )
    binned = lax.dot_general(
        stacked, lower_hot, (((1,), (1,)), ((), ())), precision=HIGHEST,
        preferred_element_type=jnp.float32,
    )
    num = binned[:uppers].reshape(owners, TILE)
    wgt = binned[uppers:].reshape(owners, TILE)
    return jnp.concatenate([num, wgt], axis=1)


def shards(tod, templates, det_weight, pixel, hitlist, counts):
    dets, samp_local = tod.shape[1], tod.shape[2]
    owners = hitlist.shape[1]
    slots = hitlist.shape[2]
    per_det = samp_local // BL
    blocks = dets * per_det

    template_rows = templates[0]
    streams = tod[0]
    gram_sum = lax.dot_general(
        template_rows, template_rows, (((1,), (1,)), ((), ())),
        precision=HIGHEST, preferred_element_type=jnp.float32,
    )
    projection = lax.dot_general(
        template_rows, streams, (((1,), (1,)), ((), ())),
        precision=HIGHEST, preferred_element_type=jnp.float32,
    )
    joined = all_sum(jnp.concatenate([gram_sum, projection], axis=1), ("section", "sub"))
    gram_sum, projection = joined[:, : gram_sum.shape[1]], joined[:, gram_sum.shape[1] :]
    factor = jnp.linalg.cholesky(gram_sum)
    coef_fit = jax.scipy.linalg.cho_solve((factor, True), projection)
    removed = lax.dot_general(
        coef_fit, template_rows, (((0,), (0,)), ((), ())),
        precision=HIGHEST, preferred_element_type=jnp.float32,
    )
    filtered = streams - removed
    weighted = filtered * det_weight[:, None]
    sample_weight = jnp.broadcast_to(det_weight[:, None], streams.shape)

    slot_ids = lax.broadcasted_iota(jnp.int32, (owners, slots), 1)
    live = slot_ids < counts[0]
    named = (hitlist[0][:, :, None] == lax.broadcasted_iota(jnp.int32, (1, 1, blocks), 2)) & live[:, :, None]
    in_tile = jnp.any(named, axis=1)
    tile_ids = lax.broadcasted_iota(jnp.int32, (owners, blocks), 0)
    tile_of_block = jnp.where(jnp.any(in_tile, axis=0), jnp.sum(jnp.where(in_tile, tile_ids, 0), axis=0), -1)
    tile_of_sample = jnp.repeat(tile_of_block.reshape(dets, per_det), BL, axis=1)

    partial = bin_tiles(weighted, pixel[0], sample_weight, tile_of_sample, owners)
    got = lax.all_to_all(partial, ("wafer", "sub"), split_axis=0, concat_axis=0, tiled=True)
    tile_sum = all_sum(jnp.sum(got, axis=0), ("section",))
    num_tile, wgt_tile = tile_sum[:TILE], tile_sum[TILE:]
    return num_tile / jnp.maximum(wgt_tile, 1.0)


def solution(mesh):
    placed = (
        P(None, "wafer", ("section", "sub")),
        P(None, "wafer", ("section", "sub")),
        P("wafer"),
        P(None, "wafer", ("section", "sub")),
        P(None, "wafer", ("section", "sub")),
        P(None, "wafer", ("section", "sub")),
    )
    return jax.shard_map(
        shards, mesh=mesh, in_specs=placed, out_specs=P(("wafer", "sub")), check_vma=False
    )
```

```python
import jax
import jax.numpy as jnp
from jax import lax
from jax.sharding import PartitionSpec as P

BL = 128
TILE = 512
HIGHEST = lax.Precision.HIGHEST


def all_sum(x, axes):
    for axis in axes:
        size = lax.axis_size(axis)
        bit = 1
        while bit < size:
            x = x + lax.ppermute(x, axis, [(i, i ^ bit) for i in range(size)])
            bit *= 2
    return x


def split_bf16(x, parts):
    pieces = []
    for _ in range(parts):
        head = lax.reduce_precision(x, exponent_bits=8, mantissa_bits=7)
        pieces.append(head.astype(jnp.bfloat16))
        x = x - head
    return pieces


def bin_tiles(values, pixels, weights, tile_of_sample, owners):
    uppers = owners * (TILE // 128)
    upper = jnp.where(tile_of_sample >= 0, tile_of_sample * (TILE // 128) + pixels // 128, -1).reshape(-1)
    lower = (pixels % 128).reshape(-1)
    count = upper.shape[0]
    upper_hot = lax.broadcasted_iota(jnp.int32, (uppers, count), 0) == upper[None, :]
    lower_hot = (lax.broadcasted_iota(jnp.int32, (128, count), 0) == lower[None, :]).astype(jnp.bfloat16)
    pieces = split_bf16(values.reshape(1, -1), 3) + split_bf16(weights.reshape(1, -1), 3)
    stacked = jnp.concatenate([jnp.where(upper_hot, p, jnp.bfloat16(0)) for p in pieces], axis=0)
    binned = lax.dot_general(
        stacked, lower_hot, (((1,), (1,)), ((), ())), preferred_element_type=jnp.float32,
    ).reshape(6, uppers, 128)
    num = ((binned[0] + binned[1]) + binned[2]).reshape(owners, TILE)
    wgt = ((binned[3] + binned[4]) + binned[5]).reshape(owners, TILE)
    return jnp.concatenate([num, wgt], axis=1)


def shards(tod, templates, det_weight, pixel, hitlist, counts):
    dets, samp_local = tod.shape[1], tod.shape[2]
    owners = hitlist.shape[1]
    slots = hitlist.shape[2]
    per_det = samp_local // BL
    blocks = dets * per_det

    template_rows = templates[0]
    streams = tod[0]
    gram_sum = lax.dot_general(
        template_rows, template_rows, (((1,), (1,)), ((), ())),
        precision=HIGHEST, preferred_element_type=jnp.float32,
    )
    projection = lax.dot_general(
        template_rows, streams, (((1,), (1,)), ((), ())),
        precision=HIGHEST, preferred_element_type=jnp.float32,
    )
    joined = all_sum(jnp.concatenate([gram_sum, projection], axis=1), ("section", "sub"))
    gram_sum, projection = joined[:, : gram_sum.shape[1]], joined[:, gram_sum.shape[1] :]
    factor = jnp.linalg.cholesky(gram_sum)
    coef_fit = jax.scipy.linalg.cho_solve((factor, True), projection)
    removed = lax.dot_general(
        coef_fit, template_rows, (((0,), (0,)), ((), ())),
        precision=HIGHEST, preferred_element_type=jnp.float32,
    )
    filtered = streams - removed
    weighted = filtered * det_weight[:, None]
    sample_weight = jnp.broadcast_to(det_weight[:, None], streams.shape)

    slot_ids = lax.broadcasted_iota(jnp.int32, (owners, slots), 1)
    live = slot_ids < counts[0]
    named = (hitlist[0][:, :, None] == lax.broadcasted_iota(jnp.int32, (1, 1, blocks), 2)) & live[:, :, None]
    in_tile = jnp.any(named, axis=1)
    tile_ids = lax.broadcasted_iota(jnp.int32, (owners, blocks), 0)
    tile_of_block = jnp.where(jnp.any(in_tile, axis=0), jnp.sum(jnp.where(in_tile, tile_ids, 0), axis=0), -1)
    tile_of_sample = jnp.repeat(tile_of_block.reshape(dets, per_det), BL, axis=1)

    partial = bin_tiles(weighted, pixel[0], sample_weight, tile_of_sample, owners)
    got = lax.all_to_all(partial, ("wafer", "sub"), split_axis=0, concat_axis=0, tiled=True)
    tile_sum = all_sum(jnp.sum(got, axis=0), ("section",))
    num_tile, wgt_tile = tile_sum[:TILE], tile_sum[TILE:]
    return num_tile / jnp.maximum(wgt_tile, 1.0)


def solution(mesh):
    placed = (
        P(None, "wafer", ("section", "sub")),
        P(None, "wafer", ("section", "sub")),
        P("wafer"),
        P(None, "wafer", ("section", "sub")),
        P(None, "wafer", ("section", "sub")),
        P(None, "wafer", ("section", "sub")),
    )
    return jax.shard_map(
        shards, mesh=mesh, in_specs=placed, out_specs=P(("wafer", "sub")), check_vma=False
    )
```

```python
import jax
import jax.numpy as jnp
from jax import lax
from jax.sharding import PartitionSpec as P

BL = 128
TILE = 512
HIGHEST = lax.Precision.HIGHEST


def partner_rounds(axis):
    size = lax.axis_size(axis)
    if axis == "section":
        chips = size // 2
        yield [(i, i ^ 1) for i in range(size)]
        inner = 2
    else:
        chips = size
        inner = 1
    if chips == 4:
        yield [(i, i ^ inner) for i in range(size)]
        yield [(i, (3 - i // inner) * inner + i % inner) for i in range(size)]
    else:
        bit = inner
        while bit < size:
            yield [(i, i ^ bit) for i in range(size)]
            bit *= 2


def all_sum(x, axes):
    for axis in axes:
        for pairs in partner_rounds(axis):
            x = x + lax.ppermute(x, axis, pairs)
    return x


def split_bf16(x, parts):
    pieces = []
    for _ in range(parts):
        head = lax.reduce_precision(x, exponent_bits=8, mantissa_bits=7)
        pieces.append(head.astype(jnp.bfloat16))
        x = x - head
    return pieces


def bin_tiles(values, pixels, weights, tile_of_sample, owners):
    uppers = owners * (TILE // 128)
    upper = jnp.where(tile_of_sample >= 0, tile_of_sample * (TILE // 128) + pixels // 128, -1).reshape(-1)
    lower = (pixels % 128).reshape(-1)
    count = upper.shape[0]
    upper_hot = lax.broadcasted_iota(jnp.int32, (uppers, count), 0) == upper[None, :]
    lower_hot = (lax.broadcasted_iota(jnp.int32, (128, count), 0) == lower[None, :]).astype(jnp.bfloat16)
    pieces = split_bf16(values.reshape(1, -1), 3) + split_bf16(weights.reshape(1, -1), 3)
    stacked = jnp.concatenate([jnp.where(upper_hot, p, jnp.bfloat16(0)) for p in pieces], axis=0)
    binned = lax.dot_general(
        stacked, lower_hot, (((1,), (1,)), ((), ())), preferred_element_type=jnp.float32,
    ).reshape(6, uppers, 128)
    num = ((binned[0] + binned[1]) + binned[2]).reshape(owners, TILE)
    wgt = ((binned[3] + binned[4]) + binned[5]).reshape(owners, TILE)
    return jnp.concatenate([num, wgt], axis=1)


def shards(tod, templates, det_weight, pixel, hitlist, counts):
    dets, samp_local = tod.shape[1], tod.shape[2]
    owners = hitlist.shape[1]
    slots = hitlist.shape[2]
    per_det = samp_local // BL
    blocks = dets * per_det

    template_rows = templates[0]
    streams = tod[0]
    gram_sum = lax.dot_general(
        template_rows, template_rows, (((1,), (1,)), ((), ())),
        precision=HIGHEST, preferred_element_type=jnp.float32,
    )
    projection = lax.dot_general(
        template_rows, streams, (((1,), (1,)), ((), ())),
        precision=HIGHEST, preferred_element_type=jnp.float32,
    )
    joined = all_sum(jnp.concatenate([gram_sum, projection], axis=1), ("section", "sub"))
    gram_sum, projection = joined[:, : gram_sum.shape[1]], joined[:, gram_sum.shape[1] :]
    factor = jnp.linalg.cholesky(gram_sum)
    coef_fit = jax.scipy.linalg.cho_solve((factor, True), projection)
    removed = lax.dot_general(
        coef_fit, template_rows, (((0,), (0,)), ((), ())),
        precision=HIGHEST, preferred_element_type=jnp.float32,
    )
    filtered = streams - removed
    weighted = filtered * det_weight[:, None]
    sample_weight = jnp.broadcast_to(det_weight[:, None], streams.shape)

    slot_ids = lax.broadcasted_iota(jnp.int32, (owners, slots), 1)
    live = slot_ids < counts[0]
    named = (hitlist[0][:, :, None] == lax.broadcasted_iota(jnp.int32, (1, 1, blocks), 2)) & live[:, :, None]
    in_tile = jnp.any(named, axis=1)
    tile_ids = lax.broadcasted_iota(jnp.int32, (owners, blocks), 0)
    tile_of_block = jnp.where(jnp.any(in_tile, axis=0), jnp.sum(jnp.where(in_tile, tile_ids, 0), axis=0), -1)
    tile_of_sample = jnp.repeat(tile_of_block.reshape(dets, per_det), BL, axis=1)

    partial = bin_tiles(weighted, pixel[0], sample_weight, tile_of_sample, owners)
    got = lax.all_to_all(partial, ("wafer", "sub"), split_axis=0, concat_axis=0, tiled=True)
    tile_sum = all_sum(jnp.sum(got, axis=0), ("section",))
    num_tile, wgt_tile = tile_sum[:TILE], tile_sum[TILE:]
    return num_tile / jnp.maximum(wgt_tile, 1.0)


def solution(mesh):
    placed = (
        P(None, "wafer", ("section", "sub")),
        P(None, "wafer", ("section", "sub")),
        P("wafer"),
        P(None, "wafer", ("section", "sub")),
        P(None, "wafer", ("section", "sub")),
        P(None, "wafer", ("section", "sub")),
    )
    return jax.shard_map(
        shards, mesh=mesh, in_specs=placed, out_specs=P(("wafer", "sub")), check_vma=False
    )
```

```python
import jax
import jax.numpy as jnp
from jax import lax
from jax.experimental import pallas as pl
from jax.experimental.pallas import tpu as pltpu
from jax.sharding import PartitionSpec as P

BL = 128
TILE = 512
HIGHEST = lax.Precision.HIGHEST


def partner_rounds(axis):
    size = lax.axis_size(axis)
    if axis == "section":
        chips = size // 2
        yield [(i, i ^ 1) for i in range(size)]
        inner = 2
    else:
        chips = size
        inner = 1
    if chips == 4:
        yield [(i, i ^ inner) for i in range(size)]
        yield [(i, (3 - i // inner) * inner + i % inner) for i in range(size)]
    else:
        bit = inner
        while bit < size:
            yield [(i, i ^ bit) for i in range(size)]
            bit *= 2


def all_sum(x, axes):
    for axis in axes:
        for pairs in partner_rounds(axis):
            x = x + lax.ppermute(x, axis, pairs)
    return x


def split_bf16(x, parts):
    pieces = []
    for _ in range(parts):
        head = lax.reduce_precision(x, exponent_bits=8, mantissa_bits=7)
        pieces.append(head.astype(jnp.bfloat16))
        x = x - head
    return pieces


def bin_tiles(values, pixels, weights, tile_of_sample, owners):
    uppers = owners * (TILE // 128)
    upper = jnp.where(tile_of_sample >= 0, tile_of_sample * (TILE // 128) + pixels // 128, -1).reshape(-1)
    lower = (pixels % 128).reshape(-1)
    count = upper.shape[0]
    upper_hot = lax.broadcasted_iota(jnp.int32, (uppers, count), 0) == upper[None, :]
    lower_hot = (lax.broadcasted_iota(jnp.int32, (128, count), 0) == lower[None, :]).astype(jnp.bfloat16)
    pieces = split_bf16(values.reshape(1, -1), 3) + split_bf16(weights.reshape(1, -1), 3)
    stacked = jnp.concatenate([jnp.where(upper_hot, p, jnp.bfloat16(0)) for p in pieces], axis=0)
    binned = lax.dot_general(
        stacked, lower_hot, (((1,), (1,)), ((), ())), preferred_element_type=jnp.float32,
    ).reshape(6, uppers, 128)
    num = ((binned[0] + binned[1]) + binned[2]).reshape(owners, TILE)
    wgt = ((binned[3] + binned[4]) + binned[5]).reshape(owners, TILE)
    return jnp.concatenate([num, wgt], axis=1)


def solve_kernel(joined_ref, coef_ref):
    n = joined_ref.shape[0]
    m = joined_ref[...]
    rows = lax.broadcasted_iota(jnp.int32, m.shape, 0)
    for k in range(n):
        row = m[k : k + 1, :]
        inv_root = 1.0 / jnp.sqrt(row[:, k : k + 1])
        scaled = row * inv_root
        column = m[:, k : k + 1] * inv_root
        m = jnp.where(rows == k, scaled, m - column * scaled)
    lanes = lax.broadcasted_iota(jnp.int32, (n, n), 1)
    diag = jnp.sum(jnp.where(lanes == rows[:, :n], m[:, :n], 0.0), axis=1, keepdims=True)
    coef_ref[...] = m[:, n:] / diag


def solve_fit(joined):
    n = joined.shape[0]
    return pl.pallas_call(
        solve_kernel,
        out_shape=jax.ShapeDtypeStruct((n, joined.shape[1] - n), jnp.float32),
        in_specs=[pl.BlockSpec(memory_space=pltpu.VMEM)],
        out_specs=pl.BlockSpec(memory_space=pltpu.VMEM),
    )(joined)


def shards(tod, templates, det_weight, pixel, hitlist, counts):
    dets, samp_local = tod.shape[1], tod.shape[2]
    owners = hitlist.shape[1]
    slots = hitlist.shape[2]
    per_det = samp_local // BL
    blocks = dets * per_det

    template_rows = templates[0]
    streams = tod[0]
    gram_sum = lax.dot_general(
        template_rows, template_rows, (((1,), (1,)), ((), ())),
        precision=HIGHEST, preferred_element_type=jnp.float32,
    )
    projection = lax.dot_general(
        template_rows, streams, (((1,), (1,)), ((), ())),
        precision=HIGHEST, preferred_element_type=jnp.float32,
    )
    joined = all_sum(jnp.concatenate([gram_sum, projection], axis=1), ("section", "sub"))
    coef_fit = solve_fit(joined)
    removed = lax.dot_general(
        coef_fit, template_rows, (((0,), (0,)), ((), ())),
        precision=HIGHEST, preferred_element_type=jnp.float32,
    )
    filtered = streams - removed
    weighted = filtered * det_weight[:, None]
    sample_weight = jnp.broadcast_to(det_weight[:, None], streams.shape)

    slot_ids = lax.broadcasted_iota(jnp.int32, (owners, slots), 1)
    live = slot_ids < counts[0]
    named = (hitlist[0][:, :, None] == lax.broadcasted_iota(jnp.int32, (1, 1, blocks), 2)) & live[:, :, None]
    in_tile = jnp.any(named, axis=1)
    tile_ids = lax.broadcasted_iota(jnp.int32, (owners, blocks), 0)
    tile_of_block = jnp.where(jnp.any(in_tile, axis=0), jnp.sum(jnp.where(in_tile, tile_ids, 0), axis=0), -1)
    tile_of_sample = jnp.repeat(tile_of_block.reshape(dets, per_det), BL, axis=1)

    partial = bin_tiles(weighted, pixel[0], sample_weight, tile_of_sample, owners)
    got = lax.all_to_all(partial, ("wafer", "sub"), split_axis=0, concat_axis=0, tiled=True)
    tile_sum = all_sum(jnp.sum(got, axis=0), ("section",))
    num_tile, wgt_tile = tile_sum[:TILE], tile_sum[TILE:]
    return num_tile / jnp.maximum(wgt_tile, 1.0)


def solution(mesh):
    placed = (
        P(None, "wafer", ("section", "sub")),
        P(None, "wafer", ("section", "sub")),
        P("wafer"),
        P(None, "wafer", ("section", "sub")),
        P(None, "wafer", ("section", "sub")),
        P(None, "wafer", ("section", "sub")),
    )
    return jax.shard_map(
        shards, mesh=mesh, in_specs=placed, out_specs=P(("wafer", "sub")), check_vma=False
    )
```

```python
import jax
import jax.numpy as jnp
from jax import lax
from jax.experimental import pallas as pl
from jax.experimental.pallas import tpu as pltpu
from jax.sharding import PartitionSpec as P

BL = 128
TILE = 512
HIGHEST = lax.Precision.HIGHEST


def partner_rounds(axis):
    size = lax.axis_size(axis)
    if axis == "section":
        chips = size // 2
        yield [(i, i ^ 1) for i in range(size)]
        inner = 2
    else:
        chips = size
        inner = 1
    if chips == 4:
        yield [(i, i ^ inner) for i in range(size)]
        yield [(i, (3 - i // inner) * inner + i % inner) for i in range(size)]
    else:
        bit = inner
        while bit < size:
            yield [(i, i ^ bit) for i in range(size)]
            bit *= 2


def all_sum(x, axes, cover=None, cover_round=0):
    rounds = [(axis, pairs) for axis in axes for pairs in partner_rounds(axis)]
    covered = None
    for index, (axis, pairs) in enumerate(rounds):
        if cover is not None and index == cover_round:
            x, covered = lax.optimization_barrier((x, cover()))
        x = x + lax.ppermute(x, axis, pairs)
    return x, covered


def split_bf16(x, parts):
    pieces = []
    for _ in range(parts):
        head = lax.reduce_precision(x, exponent_bits=8, mantissa_bits=7)
        pieces.append(head.astype(jnp.bfloat16))
        x = x - head
    return pieces


def bin_tiles(quantity, upper_hot, lower_hot, owners):
    pieces = split_bf16(quantity.reshape(1, -1), 3)
    stacked = jnp.concatenate([jnp.where(upper_hot, p, jnp.bfloat16(0)) for p in pieces], axis=0)
    binned = lax.dot_general(
        stacked, lower_hot, (((1,), (1,)), ((), ())), preferred_element_type=jnp.float32,
    ).reshape(3, upper_hot.shape[0], 128)
    return ((binned[0] + binned[1]) + binned[2]).reshape(owners, TILE)


def solve_kernel(joined_ref, coef_ref):
    n = joined_ref.shape[0]
    m = joined_ref[...]
    rows = lax.broadcasted_iota(jnp.int32, m.shape, 0)
    for k in range(n):
        row = m[k : k + 1, :]
        inv_root = 1.0 / jnp.sqrt(row[:, k : k + 1])
        scaled = row * inv_root
        column = m[:, k : k + 1] * inv_root
        m = jnp.where(rows == k, scaled, m - column * scaled)
    lanes = lax.broadcasted_iota(jnp.int32, (n, n), 1)
    diag = jnp.sum(jnp.where(lanes == rows[:, :n], m[:, :n], 0.0), axis=1, keepdims=True)
    coef_ref[...] = m[:, n:] / diag


def solve_fit(joined):
    n = joined.shape[0]
    return pl.pallas_call(
        solve_kernel,
        out_shape=jax.ShapeDtypeStruct((n, joined.shape[1] - n), jnp.float32),
        in_specs=[pl.BlockSpec(memory_space=pltpu.VMEM)],
        out_specs=pl.BlockSpec(memory_space=pltpu.VMEM),
    )(joined)


def shards(tod, templates, det_weight, pixel, hitlist, counts):
    dets, samp_local = tod.shape[1], tod.shape[2]
    owners = hitlist.shape[1]
    slots = hitlist.shape[2]
    per_det = samp_local // BL
    blocks = dets * per_det

    slot_ids = lax.broadcasted_iota(jnp.int32, (owners, slots), 1)
    live = slot_ids < counts[0]
    named = (hitlist[0][:, :, None] == lax.broadcasted_iota(jnp.int32, (1, 1, blocks), 2)) & live[:, :, None]
    in_tile = jnp.any(named, axis=1)
    tile_ids = lax.broadcasted_iota(jnp.int32, (owners, blocks), 0)
    tile_of_block = jnp.where(jnp.any(in_tile, axis=0), jnp.sum(jnp.where(in_tile, tile_ids, 0), axis=0), -1)
    tile_of_sample = jnp.repeat(tile_of_block.reshape(dets, per_det), BL, axis=1)

    uppers = owners * (TILE // 128)
    upper = jnp.where(tile_of_sample >= 0, tile_of_sample * (TILE // 128) + pixel[0] // 128, -1).reshape(1, -1)
    lower = (pixel[0] % 128).reshape(1, -1)
    upper_hot = lax.broadcasted_iota(jnp.int32, (uppers, upper.shape[1]), 0) == upper
    lower_hot = (lax.broadcasted_iota(jnp.int32, (128, upper.shape[1]), 0) == lower).astype(jnp.bfloat16)
    sample_weight = jnp.broadcast_to(det_weight[:, None], tod.shape[1:])
    template_rows = templates[0]
    streams = tod[0]
    gram_sum = lax.dot_general(
        template_rows, template_rows, (((1,), (1,)), ((), ())),
        precision=HIGHEST, preferred_element_type=jnp.float32,
    )
    projection = lax.dot_general(
        template_rows, streams, (((1,), (1,)), ((), ())),
        precision=HIGHEST, preferred_element_type=jnp.float32,
    )
    joined, wgt_part = all_sum(
        jnp.concatenate([gram_sum, projection], axis=1), ("section", "sub"),
        cover=lambda: bin_tiles(sample_weight, upper_hot, lower_hot, owners), cover_round=4,
    )
    coef_fit = solve_fit(joined)
    removed = lax.dot_general(
        coef_fit, template_rows, (((0,), (0,)), ((), ())),
        precision=HIGHEST, preferred_element_type=jnp.float32,
    )
    filtered = streams - removed
    weighted = filtered * det_weight[:, None]

    num_part = bin_tiles(weighted, upper_hot, lower_hot, owners)
    partial = jnp.concatenate([num_part, wgt_part], axis=1)
    got = lax.all_to_all(partial, ("wafer", "sub"), split_axis=0, concat_axis=0, tiled=True)
    tile_sum, _ = all_sum(jnp.sum(got, axis=0), ("section",))
    num_tile, wgt_tile = tile_sum[:TILE], tile_sum[TILE:]
    return num_tile / jnp.maximum(wgt_tile, 1.0)


def solution(mesh):
    placed = (
        P(None, "wafer", ("section", "sub")),
        P(None, "wafer", ("section", "sub")),
        P("wafer"),
        P(None, "wafer", ("section", "sub")),
        P(None, "wafer", ("section", "sub")),
        P(None, "wafer", ("section", "sub")),
    )
    return jax.shard_map(
        shards, mesh=mesh, in_specs=placed, out_specs=P(("wafer", "sub")), check_vma=False
    )
```

```python
import jax
import jax.numpy as jnp
from jax import lax
from jax.experimental import pallas as pl
from jax.experimental.pallas import tpu as pltpu
from jax.sharding import PartitionSpec as P


BL = 128
TILE = 512
HIGHEST = lax.Precision.HIGHEST


def partner_rounds(axis):
    size = lax.axis_size(axis)
    if axis == "section":
        chips = size // 2
        yield [(i, i ^ 1) for i in range(size)]
        inner = 2
    else:
        chips = size
        inner = 1
    if chips == 4:
        yield [(i, i ^ inner) for i in range(size)]
        yield [(i, (3 - i // inner) * inner + i % inner) for i in range(size)]
    else:
        bit = inner
        while bit < size:
            yield [(i, i ^ bit) for i in range(size)]
            bit *= 2


def all_sum(x, axes, cover=None, cover_round=0):
    rounds = [(axis, pairs) for axis in axes for pairs in partner_rounds(axis)]
    covered = None
    for index, (axis, pairs) in enumerate(rounds):
        if cover is not None and index == cover_round:
            x, covered = lax.optimization_barrier((x, cover()))
        x = x + lax.ppermute(x, axis, pairs)
    return x, covered


def split_bf16(x, parts):
    pieces = []
    for _ in range(parts):
        head = lax.reduce_precision(x, exponent_bits=8, mantissa_bits=7)
        pieces.append(head.astype(jnp.bfloat16))
        x = x - head
    return pieces


def bin_tiles(quantity, upper_hot, lower_hot, owners):
    pieces = split_bf16(quantity.reshape(1, -1), 3)
    stacked = jnp.concatenate([jnp.where(upper_hot, p, jnp.bfloat16(0)) for p in pieces], axis=0)
    binned = lax.dot_general(
        stacked, lower_hot, (((1,), (1,)), ((), ())), preferred_element_type=jnp.float32,
    ).reshape(3, upper_hot.shape[0], 128)
    return ((binned[0] + binned[1]) + binned[2]).reshape(owners, TILE)


def fit_kernel(joined_ref, templates_ref, streams_ref, weight_ref, weighted_ref):
    n = joined_ref.shape[0]
    m = joined_ref[...]
    rows = lax.broadcasted_iota(jnp.int32, m.shape, 0)
    for k in range(n):
        row = m[k : k + 1, :]
        inv_root = 1.0 / jnp.sqrt(row[:, k : k + 1])
        scaled = row * inv_root
        column = m[:, k : k + 1] * inv_root
        m = jnp.where(rows == k, scaled, m - column * scaled)
    lanes = lax.broadcasted_iota(jnp.int32, (n, n), 1)
    diag = jnp.sum(jnp.where(lanes == rows[:, :n], m[:, :n], 0.0), axis=1, keepdims=True)
    coef = m[:, n:] / diag
    removed = lax.dot_general(
        coef, templates_ref[...], (((0,), (0,)), ((), ())),
        precision=HIGHEST, preferred_element_type=jnp.float32,
    )
    weighted_ref[...] = (streams_ref[...] - removed) * weight_ref[...]


def fit_and_weight(joined, template_rows, streams, det_weight):
    return pl.pallas_call(
        fit_kernel,
        out_shape=jax.ShapeDtypeStruct(streams.shape, jnp.float32),
        in_specs=[pl.BlockSpec(memory_space=pltpu.VMEM)] * 4,
        out_specs=pl.BlockSpec(memory_space=pltpu.VMEM),
    )(joined, template_rows, streams, det_weight.reshape(-1, 1))


def filter_and_bin(tod, templates, det_weight, pixel, hitlist, counts):
    dets, samp_local = tod.shape[1], tod.shape[2]
    owners = hitlist.shape[1]
    slots = hitlist.shape[2]
    per_det = samp_local // BL
    blocks = dets * per_det

    slot_ids = lax.broadcasted_iota(jnp.int32, (owners, slots), 1)
    live = slot_ids < counts[0]
    named = (hitlist[0][:, :, None] == lax.broadcasted_iota(jnp.int32, (1, 1, blocks), 2)) & live[:, :, None]
    in_tile = jnp.any(named, axis=1)
    tile_ids = lax.broadcasted_iota(jnp.int32, (owners, blocks), 0)
    tile_of_block = jnp.where(jnp.any(in_tile, axis=0), jnp.sum(jnp.where(in_tile, tile_ids, 0), axis=0), -1)
    tile_of_sample = jnp.repeat(tile_of_block.reshape(dets, per_det), BL, axis=1)

    uppers = owners * (TILE // 128)
    upper = jnp.where(tile_of_sample >= 0, tile_of_sample * (TILE // 128) + pixel[0] // 128, -1).reshape(1, -1)
    lower = (pixel[0] % 128).reshape(1, -1)
    upper_hot = lax.broadcasted_iota(jnp.int32, (uppers, upper.shape[1]), 0) == upper
    lower_hot = (lax.broadcasted_iota(jnp.int32, (128, upper.shape[1]), 0) == lower).astype(jnp.bfloat16)
    sample_weight = jnp.broadcast_to(det_weight[:, None], tod.shape[1:])
    template_rows = templates[0]
    streams = tod[0]
    gram_sum = lax.dot_general(
        template_rows, template_rows, (((1,), (1,)), ((), ())),
        precision=HIGHEST, preferred_element_type=jnp.float32,
    )
    projection = lax.dot_general(
        template_rows, streams, (((1,), (1,)), ((), ())),
        precision=HIGHEST, preferred_element_type=jnp.float32,
    )
    def weight_map():
        return bin_tiles(sample_weight, upper_hot, lower_hot, owners)

    joined, wgt_part = all_sum(
        jnp.concatenate([gram_sum, projection], axis=1), ("section", "sub"),
        cover=weight_map, cover_round=4,
    )
    weighted = fit_and_weight(joined, template_rows, streams, det_weight)

    num_part = bin_tiles(weighted, upper_hot, lower_hot, owners)
    partial = jnp.concatenate([num_part, wgt_part], axis=1)
    got = lax.all_to_all(partial, ("wafer", "sub"), split_axis=0, concat_axis=0, tiled=True)
    tile_sum, _ = all_sum(jnp.sum(got, axis=0), ("section",))
    num_tile, wgt_tile = tile_sum[:TILE], tile_sum[TILE:]
    return num_tile / jnp.maximum(wgt_tile, 1.0)


def solution(mesh):
    placed = (
        P(None, "wafer", ("section", "sub")),
        P(None, "wafer", ("section", "sub")),
        P("wafer"),
        P(None, "wafer", ("section", "sub")),
        P(None, "wafer", ("section", "sub")),
        P(None, "wafer", ("section", "sub")),
    )
    return jax.shard_map(filter_and_bin, mesh=mesh, in_specs=placed, out_specs=P(("wafer", "sub")), check_vma=False)
```

```python
import jax
import jax.numpy as jnp
from jax import lax
from jax.experimental import pallas as pl
from jax.experimental.pallas import tpu as pltpu
from jax.sharding import PartitionSpec as P


BL = 128
TILE = 512
HIGHEST = lax.Precision.HIGHEST


def partner_rounds(axis):
    size = lax.axis_size(axis)
    if axis == "section":
        chips = size // 2
        yield [(i, i ^ 1) for i in range(size)]
        inner = 2
    else:
        chips = size
        inner = 1
    if chips == 4:
        yield [(i, i ^ inner) for i in range(size)]
        yield [(i, (3 - i // inner) * inner + i % inner) for i in range(size)]
    else:
        bit = inner
        while bit < size:
            yield [(i, i ^ bit) for i in range(size)]
            bit *= 2


def all_sum(x, axes, cover=None, cover_round=0):
    rounds = [(axis, pairs) for axis in axes for pairs in partner_rounds(axis)]
    covered = None
    for index, (axis, pairs) in enumerate(rounds):
        if cover is not None and index == cover_round:
            x, covered = lax.optimization_barrier((x, cover()))
        x = x + lax.ppermute(x, axis, pairs)
    if cover is not None and cover_round == len(rounds):
        x, covered = lax.optimization_barrier((x, cover()))
    return x, covered


def split_bf16(x, parts):
    pieces = []
    for _ in range(parts):
        head = lax.reduce_precision(x, exponent_bits=8, mantissa_bits=7)
        pieces.append(head.astype(jnp.bfloat16))
        x = x - head
    return pieces


def bin_tiles(quantity, upper_hot, lower_hot, owners):
    pieces = split_bf16(quantity.reshape(1, -1), 3)
    stacked = jnp.concatenate([jnp.where(upper_hot, p, jnp.bfloat16(0)) for p in pieces], axis=0)
    binned = lax.dot_general(
        stacked, lower_hot, (((1,), (1,)), ((), ())), preferred_element_type=jnp.float32,
    ).reshape(3, upper_hot.shape[0], 128)
    return ((binned[0] + binned[1]) + binned[2]).reshape(owners, TILE)


def solve_kernel(joined_ref, coef_ref):
    n = joined_ref.shape[0]
    m = joined_ref[...]
    rows = lax.broadcasted_iota(jnp.int32, m.shape, 0)
    for k in range(n):
        row = m[k : k + 1, :]
        inv_root = 1.0 / jnp.sqrt(row[:, k : k + 1])
        scaled = row * inv_root
        column = m[:, k : k + 1] * inv_root
        m = jnp.where(rows == k, scaled, m - column * scaled)
    lanes = lax.broadcasted_iota(jnp.int32, (n, n), 1)
    diag = jnp.sum(jnp.where(lanes == rows[:, :n], m[:, :n], 0.0), axis=1, keepdims=True)
    coef_ref[...] = m[:, n:] / diag


def solve_fit(joined):
    n = joined.shape[0]
    return pl.pallas_call(
        solve_kernel,
        out_shape=jax.ShapeDtypeStruct((n, joined.shape[1] - n), jnp.float32),
        in_specs=[pl.BlockSpec(memory_space=pltpu.VMEM)],
        out_specs=pl.BlockSpec(memory_space=pltpu.VMEM),
    )(joined)


def filter_and_bin(tod, templates, det_weight, pixel, hitlist, counts):
    dets, samp_local = tod.shape[1], tod.shape[2]
    owners = hitlist.shape[1]
    slots = hitlist.shape[2]
    per_det = samp_local // BL
    blocks = dets * per_det

    slot_ids = lax.broadcasted_iota(jnp.int32, (owners, slots), 1)
    live = slot_ids < counts[0]
    named = (hitlist[0][:, :, None] == lax.broadcasted_iota(jnp.int32, (1, 1, blocks), 2)) & live[:, :, None]
    in_tile = jnp.any(named, axis=1)
    tile_ids = lax.broadcasted_iota(jnp.int32, (owners, blocks), 0)
    tile_of_block = jnp.where(jnp.any(in_tile, axis=0), jnp.sum(jnp.where(in_tile, tile_ids, 0), axis=0), -1)
    tile_of_sample = jnp.repeat(tile_of_block.reshape(dets, per_det), BL, axis=1)

    uppers = owners * (TILE // 128)
    upper = jnp.where(tile_of_sample >= 0, tile_of_sample * (TILE // 128) + pixel[0] // 128, -1).reshape(1, -1)
    lower = (pixel[0] % 128).reshape(1, -1)
    upper_hot = lax.broadcasted_iota(jnp.int32, (uppers, upper.shape[1]), 0) == upper
    lower_hot = (lax.broadcasted_iota(jnp.int32, (128, upper.shape[1]), 0) == lower).astype(jnp.bfloat16)
    sample_weight = jnp.broadcast_to(det_weight[:, None], tod.shape[1:])
    template_rows = templates[0]
    streams = tod[0]
    gram_sum = lax.dot_general(
        template_rows, template_rows, (((1,), (1,)), ((), ())),
        precision=HIGHEST, preferred_element_type=jnp.float32,
    )
    projection = lax.dot_general(
        template_rows, streams, (((1,), (1,)), ((), ())),
        precision=HIGHEST, preferred_element_type=jnp.float32,
    )
    def weight_map():
        return bin_tiles(sample_weight, upper_hot, lower_hot, owners)

    joined, wgt_part = all_sum(
        jnp.concatenate([gram_sum, projection], axis=1), ("section", "sub"),
        cover=weight_map, cover_round=5,
    )
    coef_fit = solve_fit(joined)
    removed = lax.dot_general(
        coef_fit, template_rows, (((0,), (0,)), ((), ())),
        precision=HIGHEST, preferred_element_type=jnp.float32,
    )
    filtered = streams - removed
    weighted = filtered * det_weight[:, None]

    num_part = bin_tiles(weighted, upper_hot, lower_hot, owners)
    partial = jnp.concatenate([num_part, wgt_part], axis=1)
    got = lax.all_to_all(partial, ("wafer", "sub"), split_axis=0, concat_axis=0, tiled=True)
    tile_sum, _ = all_sum(jnp.sum(got, axis=0), ("section",))
    num_tile, wgt_tile = tile_sum[:TILE], tile_sum[TILE:]
    return num_tile / jnp.maximum(wgt_tile, 1.0)


def solution(mesh):
    placed = (
        P(None, "wafer", ("section", "sub")),
        P(None, "wafer", ("section", "sub")),
        P("wafer"),
        P(None, "wafer", ("section", "sub")),
        P(None, "wafer", ("section", "sub")),
        P(None, "wafer", ("section", "sub")),
    )
    return jax.shard_map(filter_and_bin, mesh=mesh, in_specs=placed, out_specs=P(("wafer", "sub")), check_vma=False)
```

```python
import jax
import jax.numpy as jnp
from jax import lax
from jax.experimental import pallas as pl
from jax.experimental.pallas import tpu as pltpu
from jax.sharding import PartitionSpec as P


BL = 128
TILE = 512
HIGHEST = lax.Precision.HIGHEST


def partner_rounds(axis):
    size = lax.axis_size(axis)
    if axis == "section":
        chips = size // 2
        yield [(i, i ^ 1) for i in range(size)]
        inner = 2
    else:
        chips = size
        inner = 1
    if chips == 4:
        yield [(i, i ^ inner) for i in range(size)]
        yield [(i, (3 - i // inner) * inner + i % inner) for i in range(size)]
    else:
        bit = inner
        while bit < size:
            yield [(i, i ^ bit) for i in range(size)]
            bit *= 2


def all_sum(x, axes, cover=None, cover_round=0):
    rounds = [(axis, pairs) for axis in axes for pairs in partner_rounds(axis)]
    covered = None
    for index, (axis, pairs) in enumerate(rounds):
        if cover is not None and index == cover_round:
            x, covered = lax.optimization_barrier((x, cover()))
        x = x + lax.ppermute(x, axis, pairs)
    if cover is not None and cover_round == len(rounds):
        x, covered = lax.optimization_barrier((x, cover()))
    return x, covered


def all_sum_split(x, axes, cover):
    rounds = [(axis, pairs) for axis in axes for pairs in partner_rounds(axis)]
    for axis, pairs in rounds[:-1]:
        x = x + lax.ppermute(x, axis, pairs)
    axis, pairs = rounds[-1]
    received = lax.ppermute(x, axis, pairs)
    return lax.optimization_barrier((x, received, cover()))


def split_bf16(x, parts):
    pieces = []
    for _ in range(parts):
        head = lax.reduce_precision(x, exponent_bits=8, mantissa_bits=7)
        pieces.append(head.astype(jnp.bfloat16))
        x = x - head
    return pieces


def bin_tiles(quantity, upper_hot, lower_hot, owners, parts):
    pieces = split_bf16(quantity[None], parts)
    stacked = jnp.concatenate([jnp.where(upper_hot, p, jnp.bfloat16(0)) for p in pieces], axis=0)
    binned = lax.dot_general(
        stacked, lower_hot, (((1, 2), (1, 2)), ((), ())), preferred_element_type=jnp.float32,
    ).reshape(parts, upper_hot.shape[0], 128)
    total = binned[parts - 1]
    for index in reversed(range(parts - 1)):
        total = binned[index] + total
    return total.reshape(owners, TILE)


def solve_kernel(own_ref, received_ref, coef_ref):
    n = own_ref.shape[0]
    m = own_ref[...] + received_ref[...]
    rows = lax.broadcasted_iota(jnp.int32, m.shape, 0)
    for k in range(n):
        row = m[k : k + 1, :]
        inv_root = 1.0 / jnp.sqrt(row[:, k : k + 1])
        scaled = row * inv_root
        column = m[:, k : k + 1] * inv_root
        m = jnp.where(rows == k, scaled, m - column * scaled)
    lanes = lax.broadcasted_iota(jnp.int32, (n, n), 1)
    diag = jnp.sum(jnp.where(lanes == rows[:, :n], m[:, :n], 0.0), axis=1, keepdims=True)
    coef_ref[...] = m[:, n:] / diag


def solve_fit(own, received):
    n = own.shape[0]
    return pl.pallas_call(
        solve_kernel,
        out_shape=jax.ShapeDtypeStruct((n, own.shape[1] - n), jnp.float32),
        in_specs=[pl.BlockSpec(memory_space=pltpu.VMEM)] * 2,
        out_specs=pl.BlockSpec(memory_space=pltpu.VMEM),
    )(own, received)


def filter_and_bin(tod, templates, det_weight, pixel, hitlist, counts):
    dets, samp_local = tod.shape[1], tod.shape[2]
    owners = hitlist.shape[1]
    slots = hitlist.shape[2]
    per_det = samp_local // BL
    blocks = dets * per_det

    slot_ids = lax.broadcasted_iota(jnp.int32, (owners, slots), 1)
    live = slot_ids < counts[0]
    named = (hitlist[0][:, :, None] == lax.broadcasted_iota(jnp.int32, (1, 1, blocks), 2)) & live[:, :, None]
    in_tile = jnp.any(named, axis=1)
    tile_ids = lax.broadcasted_iota(jnp.int32, (owners, blocks), 0)
    tile_of_block = jnp.where(jnp.any(in_tile, axis=0), jnp.sum(jnp.where(in_tile, tile_ids, 0), axis=0), -1)
    tile_of_sample = jnp.repeat(tile_of_block.reshape(dets, per_det), BL, axis=1)

    uppers = owners * (TILE // 128)
    upper = jnp.where(tile_of_sample >= 0, tile_of_sample * (TILE // 128) + pixel[0] // 128, -1)[None]
    lower = (pixel[0] % 128)[None]
    upper_hot = lax.broadcasted_iota(jnp.int32, (uppers,) + upper.shape[1:], 0) == upper
    lower_hot = (lax.broadcasted_iota(jnp.int32, (128,) + lower.shape[1:], 0) == lower).astype(jnp.bfloat16)
    sample_weight = jnp.broadcast_to(det_weight[:, None], tod.shape[1:])
    template_rows = templates[0]
    streams = tod[0]
    gram_sum = lax.dot_general(
        template_rows, template_rows, (((1,), (1,)), ((), ())),
        precision=HIGHEST, preferred_element_type=jnp.float32,
    )
    projection = lax.dot_general(
        template_rows, streams, (((1,), (1,)), ((), ())),
        precision=HIGHEST, preferred_element_type=jnp.float32,
    )
    def weight_map():
        return bin_tiles(sample_weight, upper_hot, lower_hot, owners, 3)

    own, received, wgt_part = all_sum_split(
        jnp.concatenate([gram_sum, projection], axis=1), ("section", "sub"), cover=weight_map
    )
    coef_fit = solve_fit(own, received)
    removed = lax.dot_general(
        coef_fit, template_rows, (((0,), (0,)), ((), ())),
        precision=HIGHEST, preferred_element_type=jnp.float32,
    )
    filtered = streams - removed
    weighted = filtered * det_weight[:, None]

    num_part = bin_tiles(weighted, upper_hot, lower_hot, owners, 2)
    partial = jnp.concatenate([num_part, wgt_part], axis=1)
    got = lax.all_to_all(partial, ("wafer", "sub"), split_axis=0, concat_axis=0, tiled=True)
    tile_sum, _ = all_sum(jnp.sum(got, axis=0), ("section",))
    num_tile, wgt_tile = tile_sum[:TILE], tile_sum[TILE:]
    return num_tile / jnp.maximum(wgt_tile, 1.0)


def solution(mesh):
    placed = (
        P(None, "wafer", ("section", "sub")),
        P(None, "wafer", ("section", "sub")),
        P("wafer"),
        P(None, "wafer", ("section", "sub")),
        P(None, "wafer", ("section", "sub")),
        P(None, "wafer", ("section", "sub")),
    )
    return jax.shard_map(filter_and_bin, mesh=mesh, in_specs=placed, out_specs=P(("wafer", "sub")), check_vma=False)
```

```python
import jax
import jax.numpy as jnp
from jax import lax
from jax.experimental import pallas as pl
from jax.experimental.pallas import tpu as pltpu
from jax.sharding import PartitionSpec as P


BL = 128
TILE = 512
HIGHEST = lax.Precision.HIGHEST


def partner_rounds(axis):
    size = lax.axis_size(axis)
    if axis == "section":
        chips = size // 2
        yield [(i, i ^ 1) for i in range(size)]
        inner = 2
    else:
        chips = size
        inner = 1
    if chips == 4:
        yield [(i, i ^ inner) for i in range(size)]
        yield [(i, (3 - i // inner) * inner + i % inner) for i in range(size)]
    else:
        bit = inner
        while bit < size:
            yield [(i, i ^ bit) for i in range(size)]
            bit *= 2


def all_sum(x, axes, cover=None, cover_round=0):
    rounds = [(axis, pairs) for axis in axes for pairs in partner_rounds(axis)]
    covered = None
    for index, (axis, pairs) in enumerate(rounds):
        if cover is not None and index == cover_round:
            x, covered = lax.optimization_barrier((x, cover()))
        x = x + lax.ppermute(x, axis, pairs)
    if cover is not None and cover_round == len(rounds):
        x, covered = lax.optimization_barrier((x, cover()))
    return x, covered


def all_sum_split(x, axes, cover):
    rounds = [(axis, pairs) for axis in axes for pairs in partner_rounds(axis)]
    for axis, pairs in rounds[:-1]:
        x = x + lax.ppermute(x, axis, pairs)
    axis, pairs = rounds[-1]
    received = lax.ppermute(x, axis, pairs)
    return lax.optimization_barrier((x, received, cover()))


def split_bf16(x, parts):
    pieces = []
    for _ in range(parts):
        head = lax.reduce_precision(x, exponent_bits=8, mantissa_bits=7)
        pieces.append(head.astype(jnp.bfloat16))
        x = x - head
    return pieces


def bin_tiles(quantity, upper_hot, lower_hot, owners, parts):
    pieces = split_bf16(quantity.reshape(1, -1), parts)
    stacked = jnp.concatenate([jnp.where(upper_hot, p, jnp.bfloat16(0)) for p in pieces], axis=0)
    binned = lax.dot_general(
        stacked, lower_hot, (((1,), (1,)), ((), ())), preferred_element_type=jnp.float32,
    ).reshape(parts, upper_hot.shape[0], 128)
    total = binned[parts - 1]
    for index in reversed(range(parts - 1)):
        total = binned[index] + total
    return total.reshape(owners, TILE)


def solve_kernel(own_ref, received_ref, coef_ref):
    n = own_ref.shape[0]
    m = own_ref[...] + received_ref[...]
    rows = lax.broadcasted_iota(jnp.int32, m.shape, 0)
    for k in range(n):
        row = m[k : k + 1, :]
        inv_root = 1.0 / jnp.sqrt(row[:, k : k + 1])
        scaled = row * inv_root
        column = m[:, k : k + 1] * inv_root
        m = jnp.where(rows == k, scaled, m - column * scaled)
    lanes = lax.broadcasted_iota(jnp.int32, (n, n), 1)
    diag = jnp.sum(jnp.where(lanes == rows[:, :n], m[:, :n], 0.0), axis=1, keepdims=True)
    coef_ref[...] = m[:, n:] / diag


def solve_fit(own, received):
    n = own.shape[0]
    return pl.pallas_call(
        solve_kernel,
        out_shape=jax.ShapeDtypeStruct((n, own.shape[1] - n), jnp.float32),
        in_specs=[pl.BlockSpec(memory_space=pltpu.VMEM)] * 2,
        out_specs=pl.BlockSpec(memory_space=pltpu.VMEM),
    )(own, received)


def filter_and_bin(tod, templates, det_weight, pixel, hitlist, counts):
    dets, samp_local = tod.shape[1], tod.shape[2]
    owners = hitlist.shape[1]
    slots = hitlist.shape[2]
    per_det = samp_local // BL
    blocks = dets * per_det

    slot_ids = lax.broadcasted_iota(jnp.int32, (owners, slots), 1)
    live = slot_ids < counts[0]
    named = (hitlist[0][:, :, None] == lax.broadcasted_iota(jnp.int32, (1, 1, blocks), 2)) & live[:, :, None]
    in_tile = jnp.any(named, axis=1)
    tile_ids = lax.broadcasted_iota(jnp.int32, (owners, blocks), 0)
    tile_of_block = jnp.where(jnp.any(in_tile, axis=0), jnp.sum(jnp.where(in_tile, tile_ids, 0), axis=0), -1)
    tile_of_sample = jnp.repeat(tile_of_block.reshape(dets, per_det), BL, axis=1)

    uppers = owners * (TILE // 128)
    upper = jnp.where(tile_of_sample >= 0, tile_of_sample * (TILE // 128) + pixel[0] // 128, -1).reshape(1, -1)
    lower = (pixel[0] % 128).reshape(1, -1)
    upper_hot = lax.broadcasted_iota(jnp.int32, (uppers, upper.shape[1]), 0) == upper
    lower_hot = (lax.broadcasted_iota(jnp.int32, (128, upper.shape[1]), 0) == lower).astype(jnp.bfloat16)
    sample_weight = jnp.broadcast_to(det_weight[:, None], tod.shape[1:])
    template_rows = templates[0]
    streams = tod[0]
    gram_sum = lax.dot_general(
        template_rows, template_rows, (((1,), (1,)), ((), ())),
        precision=HIGHEST, preferred_element_type=jnp.float32,
    )
    projection = lax.dot_general(
        template_rows, streams, (((1,), (1,)), ((), ())),
        precision=HIGHEST, preferred_element_type=jnp.float32,
    )
    def weight_map():
        return bin_tiles(sample_weight, upper_hot, lower_hot, owners, 2)

    own, received, wgt_part = all_sum_split(
        jnp.concatenate([gram_sum, projection], axis=1), ("section", "sub"), cover=weight_map
    )
    coef_fit = solve_fit(own, received)
    removed = lax.dot_general(
        coef_fit, template_rows, (((0,), (0,)), ((), ())),
        precision=HIGHEST, preferred_element_type=jnp.float32,
    )
    filtered = streams - removed
    weighted = filtered * det_weight[:, None]

    num_part = bin_tiles(weighted, upper_hot, lower_hot, owners, 2)
    partial = jnp.concatenate([num_part, wgt_part], axis=1)
    got = lax.all_to_all(partial, ("wafer", "sub"), split_axis=0, concat_axis=0, tiled=True)
    tile_sum, _ = all_sum(jnp.sum(got, axis=0), ("section",))
    num_tile, wgt_tile = tile_sum[:TILE], tile_sum[TILE:]
    return num_tile / jnp.maximum(wgt_tile, 1.0)


def solution(mesh):
    placed = (
        P(None, "wafer", ("section", "sub")),
        P(None, "wafer", ("section", "sub")),
        P("wafer"),
        P(None, "wafer", ("section", "sub")),
        P(None, "wafer", ("section", "sub")),
        P(None, "wafer", ("section", "sub")),
    )
    return jax.shard_map(filter_and_bin, mesh=mesh, in_specs=placed, out_specs=P(("wafer", "sub")), check_vma=False)
```

```python
import jax
import jax.numpy as jnp
from jax import lax
from jax.experimental import pallas as pl
from jax.experimental.pallas import tpu as pltpu
from jax.sharding import PartitionSpec as P


BL = 128
TILE = 512
HIGHEST = lax.Precision.HIGHEST


def partner_rounds(axis):
    size = lax.axis_size(axis)
    if axis == "section":
        chips = size // 2
        yield [(i, i ^ 1) for i in range(size)]
        inner = 2
    else:
        chips = size
        inner = 1
    if chips == 4:
        yield [(i, i ^ inner) for i in range(size)]
        yield [(i, (3 - i // inner) * inner + i % inner) for i in range(size)]
    else:
        bit = inner
        while bit < size:
            yield [(i, i ^ bit) for i in range(size)]
            bit *= 2


def all_sum(x, axes, cover=None, cover_round=0):
    rounds = [(axis, pairs) for axis in axes for pairs in partner_rounds(axis)]
    covered = None
    for index, (axis, pairs) in enumerate(rounds):
        if cover is not None and index == cover_round:
            x, covered = lax.optimization_barrier((x, cover()))
        x = x + lax.ppermute(x, axis, pairs)
    if cover is not None and cover_round == len(rounds):
        x, covered = lax.optimization_barrier((x, cover()))
    return x, covered


def all_sum_split(x, axes, cover):
    rounds = [(axis, pairs) for axis in axes for pairs in partner_rounds(axis)]
    for axis, pairs in rounds[:-1]:
        x = x + lax.ppermute(x, axis, pairs)
    axis, pairs = rounds[-1]
    received = lax.ppermute(x, axis, pairs)
    return lax.optimization_barrier((x, received, cover()))


def split_bf16(x, parts):
    pieces = []
    for _ in range(parts):
        head = lax.reduce_precision(x, exponent_bits=8, mantissa_bits=7)
        pieces.append(head.astype(jnp.bfloat16))
        x = x - head
    return pieces


def bin_tiles(quantity, upper_hot, lower_hot, owners, parts):
    pieces = split_bf16(quantity.reshape(1, -1), parts)
    stacked = jnp.concatenate([jnp.where(upper_hot, p, jnp.bfloat16(0)) for p in pieces], axis=0)
    binned = lax.dot_general(
        stacked, lower_hot, (((1,), (1,)), ((), ())), preferred_element_type=jnp.float32,
    ).reshape(parts, upper_hot.shape[0], 128)
    total = binned[parts - 1]
    for index in reversed(range(parts - 1)):
        total = binned[index] + total
    return total.reshape(owners, TILE)


def solve_kernel(own_ref, received_ref, coef_ref):
    n = own_ref.shape[0]
    m = own_ref[...] + received_ref[...]
    rows = lax.broadcasted_iota(jnp.int32, m.shape, 0)
    for k in range(n):
        row = m[k : k + 1, :]
        inv_root = 1.0 / jnp.sqrt(row[:, k : k + 1])
        scaled = row * inv_root
        column = m[:, k : k + 1] * inv_root
        m = jnp.where(rows == k, scaled, m - column * scaled)
    lanes = lax.broadcasted_iota(jnp.int32, (n, n), 1)
    diag = jnp.sum(jnp.where(lanes == rows[:, :n], m[:, :n], 0.0), axis=1, keepdims=True)
    coef_ref[...] = m[:, n:] / diag


def solve_fit(own, received):
    n = own.shape[0]
    return pl.pallas_call(
        solve_kernel,
        out_shape=jax.ShapeDtypeStruct((n, own.shape[1] - n), jnp.float32),
        in_specs=[pl.BlockSpec(memory_space=pltpu.VMEM)] * 2,
        out_specs=pl.BlockSpec(memory_space=pltpu.VMEM),
    )(own, received)


def filter_and_bin(tod, templates, det_weight, pixel, hitlist, counts):
    dets, samp_local = tod.shape[1], tod.shape[2]
    owners = hitlist.shape[1]
    slots = hitlist.shape[2]
    per_det = samp_local // BL
    blocks = dets * per_det

    slot_ids = lax.broadcasted_iota(jnp.int32, (owners, slots), 1)
    live = slot_ids < counts[0]
    named = (hitlist[0][:, :, None] == lax.broadcasted_iota(jnp.int32, (1, 1, blocks), 2)) & live[:, :, None]
    in_tile = jnp.any(named, axis=1)
    tile_ids = lax.broadcasted_iota(jnp.int32, (owners, blocks), 0)
    tile_of_block = jnp.where(jnp.any(in_tile, axis=0), jnp.sum(jnp.where(in_tile, tile_ids, 0), axis=0), -1)
    tile_of_sample = jnp.repeat(tile_of_block.reshape(dets, per_det), BL, axis=1)

    uppers = owners * (TILE // 128)
    upper = jnp.where(tile_of_sample >= 0, tile_of_sample * (TILE // 128) + pixel[0] // 128, -1).reshape(1, -1)
    lower = (pixel[0] % 128).reshape(1, -1)
    upper_hot = lax.broadcasted_iota(jnp.int32, (uppers, upper.shape[1]), 0) == upper
    lower_hot = (lax.broadcasted_iota(jnp.int32, (128, upper.shape[1]), 0) == lower).astype(jnp.bfloat16)
    sample_weight = jnp.broadcast_to(det_weight[:, None], tod.shape[1:])
    template_rows = templates[0]
    streams = tod[0]
    gram_sum = lax.dot_general(
        template_rows, template_rows, (((1,), (1,)), ((), ())),
        precision=HIGHEST, preferred_element_type=jnp.float32,
    )
    projection = lax.dot_general(
        template_rows, streams, (((1,), (1,)), ((), ())),
        precision=HIGHEST, preferred_element_type=jnp.float32,
    )
    def weight_map():
        return bin_tiles(sample_weight, upper_hot, lower_hot, owners, 3)

    own, received, wgt_part = all_sum_split(
        jnp.concatenate([gram_sum, projection], axis=1), ("section", "sub"), cover=weight_map
    )
    coef_fit = solve_fit(own, received)
    removed = lax.dot_general(
        coef_fit, template_rows, (((0,), (0,)), ((), ())),
        precision=HIGHEST, preferred_element_type=jnp.float32,
    )
    filtered = streams - removed
    weighted = filtered * det_weight[:, None]

    num_part = bin_tiles(weighted, upper_hot, lower_hot, owners, 2)
    partial = jnp.concatenate([num_part, wgt_part], axis=1)
    section_sum, _ = all_sum(partial, ("section",))
    got = lax.all_to_all(section_sum, ("wafer", "sub"), split_axis=0, concat_axis=0, tiled=True)
    tile_sum = jnp.sum(got, axis=0)
    num_tile, wgt_tile = tile_sum[:TILE], tile_sum[TILE:]
    return num_tile / jnp.maximum(wgt_tile, 1.0)


def solution(mesh):
    placed = (
        P(None, "wafer", ("section", "sub")),
        P(None, "wafer", ("section", "sub")),
        P("wafer"),
        P(None, "wafer", ("section", "sub")),
        P(None, "wafer", ("section", "sub")),
        P(None, "wafer", ("section", "sub")),
    )
    return jax.shard_map(filter_and_bin, mesh=mesh, in_specs=placed, out_specs=P(("wafer", "sub")), check_vma=False)
```

```python
import jax
import jax.numpy as jnp
from jax import lax
from jax.experimental import pallas as pl
from jax.experimental.pallas import tpu as pltpu
from jax.sharding import PartitionSpec as P


BL = 128
TILE = 512
HIGHEST = lax.Precision.HIGHEST


def partner_rounds(axis):
    size = lax.axis_size(axis)
    if axis == "section":
        chips = size // 2
        yield [(i, i ^ 1) for i in range(size)]
        inner = 2
    else:
        chips = size
        inner = 1
    if chips == 4:
        yield [(i, i ^ inner) for i in range(size)]
        yield [(i, (3 - i // inner) * inner + i % inner) for i in range(size)]
    else:
        bit = inner
        while bit < size:
            yield [(i, i ^ bit) for i in range(size)]
            bit *= 2


def all_sum(x, axes, cover=None, cover_round=0, chips_first=False):
    rounds = [(axis, pairs) for axis in axes for pairs in partner_rounds(axis)]
    if chips_first and axes == ("section",):
        rounds = rounds[1:] + rounds[:1]
    covered = None
    for index, (axis, pairs) in enumerate(rounds):
        if cover is not None and index == cover_round:
            x, covered = lax.optimization_barrier((x, cover()))
        x = x + lax.ppermute(x, axis, pairs)
    if cover is not None and cover_round == len(rounds):
        x, covered = lax.optimization_barrier((x, cover()))
    return x, covered


def all_sum_split(x, axes, cover):
    rounds = [(axis, pairs) for axis in axes for pairs in partner_rounds(axis)]
    for axis, pairs in rounds[:-1]:
        x = x + lax.ppermute(x, axis, pairs)
    axis, pairs = rounds[-1]
    received = lax.ppermute(x, axis, pairs)
    return lax.optimization_barrier((x, received, cover()))


def split_bf16(x, parts):
    pieces = []
    for _ in range(parts):
        head = lax.reduce_precision(x, exponent_bits=8, mantissa_bits=7)
        pieces.append(head.astype(jnp.bfloat16))
        x = x - head
    return pieces


def bin_tiles(quantity, upper_hot, lower_hot, owners, parts):
    pieces = split_bf16(quantity.reshape(1, -1), parts)
    stacked = jnp.concatenate([jnp.where(upper_hot, p, jnp.bfloat16(0)) for p in pieces], axis=0)
    binned = lax.dot_general(
        stacked, lower_hot, (((1,), (1,)), ((), ())), preferred_element_type=jnp.float32,
    ).reshape(parts, upper_hot.shape[0], 128)
    total = binned[parts - 1]
    for index in reversed(range(parts - 1)):
        total = binned[index] + total
    return total.reshape(owners, TILE)


def solve_kernel(own_ref, received_ref, coef_ref):
    n = own_ref.shape[0]
    m = own_ref[...] + received_ref[...]
    rows = lax.broadcasted_iota(jnp.int32, m.shape, 0)
    for k in range(n):
        row = m[k : k + 1, :]
        inv_root = 1.0 / jnp.sqrt(row[:, k : k + 1])
        scaled = row * inv_root
        column = m[:, k : k + 1] * inv_root
        m = jnp.where(rows == k, scaled, m - column * scaled)
    lanes = lax.broadcasted_iota(jnp.int32, (n, n), 1)
    diag = jnp.sum(jnp.where(lanes == rows[:, :n], m[:, :n], 0.0), axis=1, keepdims=True)
    coef_ref[...] = m[:, n:] / diag


def solve_fit(own, received):
    n = own.shape[0]
    return pl.pallas_call(
        solve_kernel,
        out_shape=jax.ShapeDtypeStruct((n, own.shape[1] - n), jnp.float32),
        in_specs=[pl.BlockSpec(memory_space=pltpu.VMEM)] * 2,
        out_specs=pl.BlockSpec(memory_space=pltpu.VMEM),
    )(own, received)


def filter_and_bin(tod, templates, det_weight, pixel, hitlist, counts):
    dets, samp_local = tod.shape[1], tod.shape[2]
    owners = hitlist.shape[1]
    slots = hitlist.shape[2]
    per_det = samp_local // BL
    blocks = dets * per_det

    slot_ids = lax.broadcasted_iota(jnp.int32, (owners, slots), 1)
    live = slot_ids < counts[0]
    named = (hitlist[0][:, :, None] == lax.broadcasted_iota(jnp.int32, (1, 1, blocks), 2)) & live[:, :, None]
    in_tile = jnp.any(named, axis=1)
    tile_ids = lax.broadcasted_iota(jnp.int32, (owners, blocks), 0)
    tile_of_block = jnp.where(jnp.any(in_tile, axis=0), jnp.sum(jnp.where(in_tile, tile_ids, 0), axis=0), -1)
    tile_of_sample = jnp.repeat(tile_of_block.reshape(dets, per_det), BL, axis=1)

    uppers = owners * (TILE // 128)
    upper = jnp.where(tile_of_sample >= 0, tile_of_sample * (TILE // 128) + pixel[0] // 128, -1).reshape(1, -1)
    lower = (pixel[0] % 128).reshape(1, -1)
    upper_hot = lax.broadcasted_iota(jnp.int32, (uppers, upper.shape[1]), 0) == upper
    lower_hot = (lax.broadcasted_iota(jnp.int32, (128, upper.shape[1]), 0) == lower).astype(jnp.bfloat16)
    sample_weight = jnp.broadcast_to(det_weight[:, None], tod.shape[1:])
    template_rows = templates[0]
    streams = tod[0]
    gram_sum = lax.dot_general(
        template_rows, template_rows, (((1,), (1,)), ((), ())),
        precision=HIGHEST, preferred_element_type=jnp.float32,
    )
    projection = lax.dot_general(
        template_rows, streams, (((1,), (1,)), ((), ())),
        precision=HIGHEST, preferred_element_type=jnp.float32,
    )
    def weight_map():
        return bin_tiles(sample_weight, upper_hot, lower_hot, owners, 3)

    own, received, wgt_part = all_sum_split(
        jnp.concatenate([gram_sum, projection], axis=1), ("section", "sub"), cover=weight_map
    )
    coef_fit = solve_fit(own, received)
    removed = lax.dot_general(
        coef_fit, template_rows, (((0,), (0,)), ((), ())),
        precision=HIGHEST, preferred_element_type=jnp.float32,
    )
    filtered = streams - removed
    weighted = filtered * det_weight[:, None]

    num_part = bin_tiles(weighted, upper_hot, lower_hot, owners, 2)
    partial = jnp.concatenate([num_part, wgt_part], axis=1)
    got = lax.all_to_all(partial, ("wafer", "sub"), split_axis=0, concat_axis=0, tiled=True)
    tile_sum, _ = all_sum(jnp.sum(got, axis=0), ("section",), chips_first=True)
    num_tile, wgt_tile = tile_sum[:TILE], tile_sum[TILE:]
    return num_tile / jnp.maximum(wgt_tile, 1.0)


def solution(mesh):
    placed = (
        P(None, "wafer", ("section", "sub")),
        P(None, "wafer", ("section", "sub")),
        P("wafer"),
        P(None, "wafer", ("section", "sub")),
        P(None, "wafer", ("section", "sub")),
        P(None, "wafer", ("section", "sub")),
    )
    return jax.shard_map(filter_and_bin, mesh=mesh, in_specs=placed, out_specs=P(("wafer", "sub")), check_vma=False)
```

```python
import jax
import jax.numpy as jnp
from jax import lax
from jax.experimental import pallas as pl
from jax.experimental.pallas import tpu as pltpu
from jax.sharding import PartitionSpec as P


BL = 128
TILE = 512
HIGHEST = lax.Precision.HIGHEST


def partner_rounds(axis):
    size = lax.axis_size(axis)
    if axis == "section":
        chips = size // 2
        yield [(i, i ^ 1) for i in range(size)]
        inner = 2
    else:
        chips = size
        inner = 1
    if chips == 4:
        yield [(i, i ^ inner) for i in range(size)]
        yield [(i, (3 - i // inner) * inner + i % inner) for i in range(size)]
    else:
        bit = inner
        while bit < size:
            yield [(i, i ^ bit) for i in range(size)]
            bit *= 2


def all_sum(x, axes, cover=None, cover_round=0):
    rounds = [(axis, pairs) for axis in axes for pairs in partner_rounds(axis)]
    covered = None
    for index, (axis, pairs) in enumerate(rounds):
        if cover is not None and index == cover_round:
            x, covered = lax.optimization_barrier((x, cover()))
        x = x + lax.ppermute(x, axis, pairs)
    if cover is not None and cover_round == len(rounds):
        x, covered = lax.optimization_barrier((x, cover()))
    return x, covered


def all_sum_split(x, axes, cover):
    rounds = [(axis, pairs) for axis in axes for pairs in partner_rounds(axis)]
    for axis, pairs in rounds[:-1]:
        x = x + lax.ppermute(x, axis, pairs)
    axis, pairs = rounds[-1]
    received = lax.ppermute(x, axis, pairs)
    return lax.optimization_barrier((x, received, cover()))


def split_bf16(x, parts):
    pieces = []
    for _ in range(parts):
        head = lax.reduce_precision(x, exponent_bits=8, mantissa_bits=7)
        pieces.append(head.astype(jnp.bfloat16))
        x = x - head
    return pieces


def bin_tiles(quantity, upper_hot, lower_hot, owners, parts):
    pieces = split_bf16(quantity.reshape(1, -1), parts)
    stacked = jnp.concatenate([jnp.where(upper_hot, p, jnp.bfloat16(0)) for p in pieces], axis=0)
    binned = lax.dot_general(
        stacked, lower_hot, (((1,), (1,)), ((), ())), preferred_element_type=jnp.float32,
    ).reshape(parts, upper_hot.shape[0], 128)
    total = binned[parts - 1]
    for index in reversed(range(parts - 1)):
        total = binned[index] + total
    return total.reshape(owners, TILE)


def solve_kernel(own_ref, received_ref, coef_ref):
    n = own_ref.shape[0]
    m = own_ref[...] + received_ref[...]
    rows = lax.broadcasted_iota(jnp.int32, m.shape, 0)
    for k in range(n):
        row = m[k : k + 1, :]
        scaled = row * (1.0 / row[:, k : k + 1])
        m = jnp.where(rows == k, scaled, m - m[:, k : k + 1] * scaled)
    coef_ref[...] = m[:, n:]


def solve_fit(own, received):
    n = own.shape[0]
    return pl.pallas_call(
        solve_kernel,
        out_shape=jax.ShapeDtypeStruct((n, own.shape[1] - n), jnp.float32),
        in_specs=[pl.BlockSpec(memory_space=pltpu.VMEM)] * 2,
        out_specs=pl.BlockSpec(memory_space=pltpu.VMEM),
    )(own, received)


def filter_and_bin(tod, templates, det_weight, pixel, hitlist, counts):
    dets, samp_local = tod.shape[1], tod.shape[2]
    owners = hitlist.shape[1]
    slots = hitlist.shape[2]
    per_det = samp_local // BL
    blocks = dets * per_det

    slot_ids = lax.broadcasted_iota(jnp.int32, (owners, slots), 1)
    live = slot_ids < counts[0]
    named = (hitlist[0][:, :, None] == lax.broadcasted_iota(jnp.int32, (1, 1, blocks), 2)) & live[:, :, None]
    in_tile = jnp.any(named, axis=1)
    tile_ids = lax.broadcasted_iota(jnp.int32, (owners, blocks), 0)
    tile_of_block = jnp.where(jnp.any(in_tile, axis=0), jnp.sum(jnp.where(in_tile, tile_ids, 0), axis=0), -1)
    tile_of_sample = jnp.repeat(tile_of_block.reshape(dets, per_det), BL, axis=1)

    uppers = owners * (TILE // 128)
    upper = jnp.where(tile_of_sample >= 0, tile_of_sample * (TILE // 128) + pixel[0] // 128, -1).reshape(1, -1)
    lower = (pixel[0] % 128).reshape(1, -1)
    upper_hot = lax.broadcasted_iota(jnp.int32, (uppers, upper.shape[1]), 0) == upper
    lower_hot = (lax.broadcasted_iota(jnp.int32, (128, upper.shape[1]), 0) == lower).astype(jnp.bfloat16)
    sample_weight = jnp.broadcast_to(det_weight[:, None], tod.shape[1:])
    template_rows = templates[0]
    streams = tod[0]
    gram_sum = lax.dot_general(
        template_rows, template_rows, (((1,), (1,)), ((), ())),
        precision=HIGHEST, preferred_element_type=jnp.float32,
    )
    projection = lax.dot_general(
        template_rows, streams, (((1,), (1,)), ((), ())),
        precision=HIGHEST, preferred_element_type=jnp.float32,
    )
    def weight_map():
        return bin_tiles(sample_weight, upper_hot, lower_hot, owners, 3)

    own, received, wgt_part = all_sum_split(
        jnp.concatenate([gram_sum, projection], axis=1), ("sub", "section"), cover=weight_map
    )
    coef_fit = solve_fit(own, received)
    removed = lax.dot_general(
        coef_fit, template_rows, (((0,), (0,)), ((), ())),
        precision=HIGHEST, preferred_element_type=jnp.float32,
    )
    filtered = streams - removed
    weighted = filtered * det_weight[:, None]

    num_part = bin_tiles(weighted, upper_hot, lower_hot, owners, 2)
    partial = jnp.concatenate([num_part, wgt_part], axis=1)
    got = lax.all_to_all(partial, ("wafer", "sub"), split_axis=0, concat_axis=0, tiled=True)
    tile_sum, _ = all_sum(jnp.sum(got, axis=0), ("section",))
    num_tile, wgt_tile = tile_sum[:TILE], tile_sum[TILE:]
    return num_tile / jnp.maximum(wgt_tile, 1.0)


def solution(mesh):
    placed = (
        P(None, "wafer", ("section", "sub")),
        P(None, "wafer", ("section", "sub")),
        P("wafer"),
        P(None, "wafer", ("section", "sub")),
        P(None, "wafer", ("section", "sub")),
        P(None, "wafer", ("section", "sub")),
    )
    return jax.shard_map(filter_and_bin, mesh=mesh, in_specs=placed, out_specs=P(("wafer", "sub")), check_vma=False)
```

```python
import jax
import jax.numpy as jnp
from jax import lax
from jax.experimental import pallas as pl
from jax.experimental.pallas import tpu as pltpu
from jax.sharding import PartitionSpec as P


BL = 128
TILE = 512
HIGHEST = lax.Precision.HIGHEST


def partner_rounds(axis):
    size = lax.axis_size(axis)
    if axis == "section":
        chips = size // 2
        yield [(i, i ^ 1) for i in range(size)]
        inner = 2
    else:
        chips = size
        inner = 1
    if chips == 4:
        yield [(i, i ^ inner) for i in range(size)]
        yield [(i, (3 - i // inner) * inner + i % inner) for i in range(size)]
    else:
        bit = inner
        while bit < size:
            yield [(i, i ^ bit) for i in range(size)]
            bit *= 2


def all_sum(x, axes, cover=None, cover_round=0):
    rounds = [(axis, pairs) for axis in axes for pairs in partner_rounds(axis)]
    covered = None
    for index, (axis, pairs) in enumerate(rounds):
        if cover is not None and index == cover_round:
            x, covered = lax.optimization_barrier((x, cover()))
        x = x + lax.ppermute(x, axis, pairs)
    if cover is not None and cover_round == len(rounds):
        x, covered = lax.optimization_barrier((x, cover()))
    return x, covered


def all_sum_split(x, axes, cover):
    rounds = [(axis, pairs) for axis in axes for pairs in partner_rounds(axis)]
    for axis, pairs in rounds[:-1]:
        x = x + lax.ppermute(x, axis, pairs)
    axis, pairs = rounds[-1]
    received = lax.ppermute(x, axis, pairs)
    return lax.optimization_barrier((x, received, cover()))


def split_bf16(x, parts):
    pieces = []
    for _ in range(parts):
        head = lax.reduce_precision(x, exponent_bits=8, mantissa_bits=7)
        pieces.append(head.astype(jnp.bfloat16))
        x = x - head
    return pieces


def bin_tiles(quantity, upper_hot, lower_hot, owners, parts):
    pieces = split_bf16(quantity.reshape(1, -1), parts)
    stacked = jnp.concatenate([jnp.where(upper_hot, p, jnp.bfloat16(0)) for p in pieces], axis=0)
    binned = lax.dot_general(
        stacked, lower_hot, (((1,), (1,)), ((), ())), preferred_element_type=jnp.float32,
    ).reshape(parts, upper_hot.shape[0], 128)
    total = binned[parts - 1]
    for index in reversed(range(parts - 1)):
        total = binned[index] + total
    return total.reshape(owners, TILE)


def solve_kernel(joined_ref, coef_ref):
    n = joined_ref.shape[0]
    m = joined_ref[...]
    rows = lax.broadcasted_iota(jnp.int32, m.shape, 0)
    for k in range(n):
        row = m[k : k + 1, :]
        scaled = row * (1.0 / row[:, k : k + 1])
        m = jnp.where(rows == k, scaled, m - m[:, k : k + 1] * scaled)
    coef_ref[...] = m[:, n:]


def solve_fit(own, received):
    n = own.shape[0]
    return pl.pallas_call(
        solve_kernel,
        out_shape=jax.ShapeDtypeStruct((n, own.shape[1] - n), jnp.float32),
        in_specs=[pl.BlockSpec(memory_space=pltpu.VMEM)],
        out_specs=pl.BlockSpec(memory_space=pltpu.VMEM),
        compiler_params=pltpu.CompilerParams(allow_input_fusion=[True]),
    )(own + received)


def filter_and_bin(tod, templates, det_weight, pixel, hitlist, counts):
    dets, samp_local = tod.shape[1], tod.shape[2]
    owners = hitlist.shape[1]
    slots = hitlist.shape[2]
    per_det = samp_local // BL
    blocks = dets * per_det

    slot_ids = lax.broadcasted_iota(jnp.int32, (owners, slots), 1)
    live = slot_ids < counts[0]
    named = (hitlist[0][:, :, None] == lax.broadcasted_iota(jnp.int32, (1, 1, blocks), 2)) & live[:, :, None]
    in_tile = jnp.any(named, axis=1)
    tile_ids = lax.broadcasted_iota(jnp.int32, (owners, blocks), 0)
    tile_of_block = jnp.where(jnp.any(in_tile, axis=0), jnp.sum(jnp.where(in_tile, tile_ids, 0), axis=0), -1)
    tile_of_sample = jnp.repeat(tile_of_block.reshape(dets, per_det), BL, axis=1)

    uppers = owners * (TILE // 128)
    upper = jnp.where(tile_of_sample >= 0, tile_of_sample * (TILE // 128) + pixel[0] // 128, -1).reshape(1, -1)
    lower = (pixel[0] % 128).reshape(1, -1)
    upper_hot = lax.broadcasted_iota(jnp.int32, (uppers, upper.shape[1]), 0) == upper
    lower_hot = (lax.broadcasted_iota(jnp.int32, (128, upper.shape[1]), 0) == lower).astype(jnp.bfloat16)
    sample_weight = jnp.broadcast_to(det_weight[:, None], tod.shape[1:])
    template_rows = templates[0]
    streams = tod[0]
    gram_sum = lax.dot_general(
        template_rows, template_rows, (((1,), (1,)), ((), ())),
        precision=HIGHEST, preferred_element_type=jnp.float32,
    )
    projection = lax.dot_general(
        template_rows, streams, (((1,), (1,)), ((), ())),
        precision=HIGHEST, preferred_element_type=jnp.float32,
    )
    def weight_map():
        return bin_tiles(sample_weight, upper_hot, lower_hot, owners, 2)

    own, received, wgt_part = all_sum_split(
        jnp.concatenate([gram_sum, projection], axis=1), ("section", "sub"), cover=weight_map
    )
    coef_fit = solve_fit(own, received)
    removed = lax.dot_general(
        coef_fit, template_rows, (((0,), (0,)), ((), ())),
        precision=HIGHEST, preferred_element_type=jnp.float32,
    )
    filtered = streams - removed
    weighted = filtered * det_weight[:, None]

    num_part = bin_tiles(weighted, upper_hot, lower_hot, owners, 2)
    partial = jnp.concatenate([num_part, wgt_part], axis=1)
    got = lax.all_to_all(partial, ("wafer", "sub"), split_axis=0, concat_axis=0, tiled=True)
    tile_sum, _ = all_sum(jnp.sum(got, axis=0), ("section",))
    num_tile, wgt_tile = tile_sum[:TILE], tile_sum[TILE:]
    return num_tile / jnp.maximum(wgt_tile, 1.0)


def solution(mesh):
    placed = (
        P(None, "wafer", ("section", "sub")),
        P(None, "wafer", ("section", "sub")),
        P("wafer"),
        P(None, "wafer", ("section", "sub")),
        P(None, "wafer", ("section", "sub")),
        P(None, "wafer", ("section", "sub")),
    )
    return jax.shard_map(filter_and_bin, mesh=mesh, in_specs=placed, out_specs=P(("wafer", "sub")), check_vma=False)
```
